768 devices in a mesh: pipe: 4 (over y_lo), dp: 48 (over y_hi, z, core), tensor: 4 (over x).
Axes of the slice: x: 4, y: 8 (y_hi: 2, y_lo: 4; y = y_hi * 4 + y_lo), z: 12, core: 2. Of those that a mesh axis runs over, the one named last changes fastest.
Arguments:
- grad_out: bfloat16 [4, 4, 48, 96, 6144], P('pipe', None, 'dp'), may hold values from -6 to 6
- qkv_saved: bfloat16 [4, 4, 48, 96, 4, 384], P('pipe', None, 'dp', None, 'tensor'), may hold values from -5 to 5
- w_out: bfloat16 [4, 6144, 4, 128], P('pipe', None, 'tensor'), may hold values from -0.078125 to 0.078125
- w_qkv: bfloat16 [4, 6144, 4, 384], P('pipe', None, 'tensor'), may hold values from -0.15625 to 0.15625
- plan: int32 [4, 4], P('pipe'), may hold values from 0 to 3, each once within a row
Outputs:
- input_grad: bfloat16 [4, 48, 96, 2, 6144], P('pipe', 'dp', 'tensor')
- out_proj_grad: float32 [4, 6144, 4, 128], P('pipe', 'dp', 'tensor')
The draws below stay inside these ranges and needn't reach their ends.
All inputs are finite; a program needn't handle non-finite values.
Results may differ from the reference program's by a relative error of at most 0.028.
Values may be sent and summed in bfloat16 or wider, within the bound.
No kernel may reach another device: no remote copies, remote signals or barrier semaphores. Data moves between devices by JAX's collectives and lax.ppermute only.
A program may use at most 64 MiB of HBM per device.

```python
from functools import reduce
import jax
import jax.numpy as jnp
from jax import lax

D = 6144
HEAD = 128
SEQ = 96
MICRO = 4
BMICRO = 2
SECTIONS = 4
SEQS = 48
HEADS = 4


def draw_qkv_saved(key, part):
    shape = (SECTIONS, MICRO, SEQS, SEQ, HEADS, 3 * HEAD)
    first_key = jax.random.fold_in(key, 11)
    entries = jnp.clip(jax.random.normal(first_key, shape, jnp.float32), -4.0, 4.0)
    return entries.astype(jnp.bfloat16)


def strengthened(result, rng, source, target, parts, factor):
    def block_of(dim):
        return (jnp.arange(result.shape[dim]) // (result.shape[dim] // parts)).reshape((-1,) + (1,) * (result.ndim - 1 - dim))

    first = jax.random.permutation(rng, parts)[block_of(target)]
    far = (block_of(target) + parts // 2) % parts
    return jnp.where((block_of(source) == first) | (block_of(source) == far), factor * result, result)


def block_scale(key, shape, shards, low, largest):
    def one(dim, parts):
        heights = jax.random.uniform(jax.random.fold_in(jax.random.fold_in(key, 6), dim), (parts,), jnp.float32, low / len(shards), largest / len(shards))
        return jnp.repeat(jnp.exp(heights), shape[dim] // parts).reshape((-1,) + (1,) * (len(shape) - dim - 1))

    level = one(*shards[0])
    for cut in shards[1:]:
        level = level * one(*cut)
    return level


def normal_values(own_key, extent, width, bound, pieces=(), held_as=jnp.bfloat16):
    values = width * jax.random.normal(own_key, extent, jnp.float32)
    if pieces:
        values = values * block_scale(own_key, extent, pieces, -0.22, 0.18)
    return jnp.clip(values, -bound, bound).astype(held_as)


def heavy_noise(key, extent, deviation, limit, split, heavy, kind=jnp.bfloat16):
    values = deviation * jax.random.normal(key, extent, jnp.float32)
    if split:
        values = values * block_scale(key, extent, split, -0.22, 0.18)
    return jnp.clip(strengthened(values, jax.random.fold_in(key, 3), *heavy), -limit, limit).astype(kind)


def setup_inputs(seed: int = 0) -> dict:
    arg_keys = jax.random.split(jax.random.key(seed), 6)
    grad_out = heavy_noise(arg_keys[0], (SECTIONS, MICRO, SEQS, SEQ, D), 1.0, 6.0, ((0, 4), (2, 48)), (2, 4, 48, 3.25))
    qkv_saved = draw_qkv_saved(jax.random.fold_in(arg_keys[5], 71), 0)
    w_out = normal_values(arg_keys[2], (SECTIONS, D, HEADS, HEAD), D ** -0.5, 0.078125, ((0, 4), (2, 4)))
    w_qkv = normal_values(arg_keys[3], (SECTIONS, D, HEADS, 3 * HEAD), (3 * HEAD * HEADS) ** -0.5, 0.15625, ((0, 4), (2, 4)))
    plan = jax.vmap(lambda own: jax.random.permutation(own, MICRO))(jax.random.split(arg_keys[4], SECTIONS)).reshape((SECTIONS, MICRO)).astype(jnp.int32)
    return {"grad_out": grad_out, "qkv_saved": qkv_saved, "w_out": w_out, "w_qkv": w_qkv, "plan": plan}


def head_forward(queries, key_rows, values):
    score_scale = HEAD ** -0.5
    scores = jnp.dot(queries, key_rows.T, preferred_element_type=jnp.float32) * score_scale
    row_ids = lax.broadcasted_iota(jnp.int32, scores.shape, 0)
    col_ids = lax.broadcasted_iota(jnp.int32, scores.shape, 1)
    scores = jnp.where(col_ids <= row_ids, scores, -1e30)
    row_max = jnp.max(scores, axis=1, keepdims=True)
    weights = jnp.exp(scores - row_max)
    softmax = weights / jnp.sum(weights, axis=1, keepdims=True)
    soft_low = softmax.astype(jnp.bfloat16)
    attended = jnp.dot(soft_low, values, preferred_element_type=jnp.float32).astype(jnp.bfloat16)
    return softmax, soft_low, attended


def head_backward(queries, key_rows, values, grad_head):
    score_scale = HEAD ** -0.5
    softmax, soft_low, attended = head_forward(queries, key_rows, values)
    row_dot = jnp.sum(grad_head.astype(jnp.float32) * attended.astype(jnp.float32), axis=1, keepdims=True)
    grad_values = jnp.dot(soft_low.T, grad_head, preferred_element_type=jnp.float32)
    grad_probs = jnp.dot(grad_head, values.T, preferred_element_type=jnp.float32)
    grad_scores = (softmax * (grad_probs - row_dot)).astype(jnp.bfloat16)
    grad_query = jnp.dot(grad_scores, key_rows, preferred_element_type=jnp.float32) * score_scale
    grad_keys = jnp.dot(grad_scores.T, queries, preferred_element_type=jnp.float32) * score_scale
    return jnp.concatenate([grad_query, grad_keys, grad_values], axis=1).astype(jnp.bfloat16)


def one_sequence(grad_seq, qkv_seq, out_proj, qkv_proj, order):
    input_parts = []
    weight_parts = []
    for head_index in range(HEADS):
        block = qkv_seq[:, :, head_index, :]
        weight_head = jnp.zeros((D, HEAD), jnp.float32)
        for micro_index in range(MICRO):
            chosen = block[micro_index]
            softmax, soft_low, attended = head_forward(chosen[:, :HEAD], chosen[:, HEAD:2 * HEAD], chosen[:, 2 * HEAD:])
            weight_head = weight_head + jnp.dot(grad_seq[micro_index].T, attended, preferred_element_type=jnp.float32)
        weight_parts.append(weight_head)
        head_terms = []
        for slot_index in range(BMICRO):
            picked = order[slot_index]
            chosen = block[picked]
            grad_rows = grad_seq[picked]
            grad_head = jnp.dot(grad_rows, out_proj[:, head_index, :], preferred_element_type=jnp.float32).astype(jnp.bfloat16)
            grad_qkv = head_backward(chosen[:, :HEAD], chosen[:, HEAD:2 * HEAD], chosen[:, 2 * HEAD:], grad_head)
            term = jnp.dot(grad_qkv, qkv_proj[:, head_index, :].T, preferred_element_type=jnp.float32).astype(jnp.bfloat16)
            term = lax.optimization_barrier(term).astype(jnp.float32)
            head_terms.append(term)
        input_parts.append(jnp.stack(head_terms, axis=1))
    summed = reduce(lambda left, right: left + right, input_parts)
    return summed.astype(jnp.bfloat16), jnp.stack(weight_parts, axis=1)


def reference(grad_out, qkv_saved, w_out, w_qkv, plan):
    def one_section(section_args):
        grad_section, qkv_section, out_proj, qkv_proj, order = section_args

        def advance(carry, seq_args):
            grad_seq, qkv_seq = seq_args
            input_seq, weight_seq = one_sequence(grad_seq, qkv_seq, out_proj, qkv_proj, order)
            return carry + weight_seq, input_seq

        start = jnp.zeros((D, HEADS, HEAD), jnp.float32)
        weight_total, inputs = lax.scan(advance, start, (jnp.moveaxis(grad_section, 1, 0), jnp.moveaxis(qkv_section, 1, 0)))
        return inputs, weight_total

    inputs, weights = lax.map(one_section, (grad_out, qkv_saved, w_out, w_qkv, plan))
    shifted = jnp.concatenate([inputs[1:], jnp.zeros_like(inputs[:1])], axis=0)
    return shifted, weights
```

```python
import jax
import jax.numpy as jnp
from jax import lax
from jax.sharding import PartitionSpec as P

BMICRO = 2


def shifted(block, axis, distance):
    devices = range(lax.axis_size(axis))
    route = [(i - distance, i) for i in devices if i - distance in devices]
    return lax.ppermute(block, axis, route)


def exchange(block, axis):
    n = lax.axis_size(axis)
    parts = block.reshape(n, block.shape[0] // n, *block.shape[1:])
    return lax.all_to_all(parts, axis, 0, 0, tiled=True).astype(jnp.float32)


def ordered_sum(parts):
    total = parts[0]
    for index in range(1, parts.shape[0]):
        total = total + parts[index]
    return total


def head_forward(queries, key_rows, values):
    score_scale = queries.shape[-1] ** (-0.5)
    scores = jnp.dot(queries, key_rows.T, preferred_element_type=jnp.float32) * score_scale
    row_ids = lax.broadcasted_iota(jnp.int32, scores.shape, 0)
    col_ids = lax.broadcasted_iota(jnp.int32, scores.shape, 1)
    scores = jnp.where(col_ids <= row_ids, scores, -1e30)
    row_max = jnp.max(scores, axis=1, keepdims=True)
    weights = jnp.exp(scores - row_max)
    softmax = weights / jnp.sum(weights, axis=1, keepdims=True)
    soft_low = softmax.astype(jnp.bfloat16)
    attended = jnp.dot(soft_low, values, preferred_element_type=jnp.float32).astype(jnp.bfloat16)
    return (softmax, soft_low, attended)


def head_backward(queries, key_rows, values, softmax, soft_low, attended, grad_head):
    score_scale = queries.shape[-1] ** (-0.5)
    row_dot = jnp.sum(
        grad_head.astype(jnp.float32) * attended.astype(jnp.float32), axis=1, keepdims=True
    )
    grad_values = jnp.dot(soft_low.T, grad_head, preferred_element_type=jnp.float32)
    grad_probs = jnp.dot(grad_head, values.T, preferred_element_type=jnp.float32)
    grad_scores = (softmax * (grad_probs - row_dot)).astype(jnp.bfloat16)
    grad_query = jnp.dot(grad_scores, key_rows, preferred_element_type=jnp.float32) * score_scale
    grad_keys = jnp.dot(grad_scores.T, queries, preferred_element_type=jnp.float32) * score_scale
    return jnp.concatenate([grad_query, grad_keys, grad_values], axis=1).astype(jnp.bfloat16)


def body(grad_out, qkv_saved, w_out, w_qkv, plan):
    gradients = grad_out[0, :, 0]
    saved_qkv = qkv_saved[0, :, 0, :, 0]
    out_proj = w_out[0, :, 0]
    qkv_proj = w_qkv[0, :, 0]
    head_size = out_proj.shape[1]
    queries = saved_qkv[:, :, :head_size]
    key_rows = saved_qkv[:, :, head_size : 2 * head_size]
    values = saved_qkv[:, :, 2 * head_size :]
    softmax, soft_low, attended = jax.vmap(head_forward)(queries, key_rows, values)
    weight_part = jnp.einsum("msc,msh->ch", gradients, attended, preferred_element_type=jnp.float32)
    weight_grad = jnp.sum(exchange(weight_part.astype(jnp.bfloat16), "dp"), axis=0)
    current = plan[0, :BMICRO]
    grad_current = jnp.take(gradients, current, axis=0)
    grad_heads = jnp.einsum(
        "msd,dh->msh", grad_current, out_proj, preferred_element_type=jnp.float32
    ).astype(jnp.bfloat16)
    grad_qkv = jax.vmap(head_backward)(
        jnp.take(queries, current, axis=0),
        jnp.take(key_rows, current, axis=0),
        jnp.take(values, current, axis=0),
        jnp.take(softmax, current, axis=0),
        jnp.take(soft_low, current, axis=0),
        jnp.take(attended, current, axis=0),
        grad_heads,
    )
    partials = jnp.einsum("bsk,dk->sbd", grad_qkv, qkv_proj, preferred_element_type=jnp.float32)
    own_rows = ordered_sum(exchange(partials.astype(jnp.bfloat16), "tensor"))
    received = shifted(own_rows.astype(jnp.bfloat16), "pipe", -1)
    return (received[None, None], weight_grad[None, :, None, :])


def solution(mesh):
    in_specs = (
        P("pipe", None, "dp", None, None),
        P("pipe", None, "dp", None, "tensor", None),
        P("pipe", None, "tensor", None),
        P("pipe", None, "tensor", None),
        P("pipe", None),
    )
    out_specs = (P("pipe", "dp", "tensor", None, None), P("pipe", "dp", "tensor", None))
    return jax.shard_map(body, mesh=mesh, in_specs=in_specs, out_specs=out_specs, check_vma=False)
```

```python
import jax
import jax.numpy as jnp
from jax import lax
from jax.sharding import Mesh, PartitionSpec as P

BMICRO = 2
DP_PARTS = ("dp_y", "dp_z", "dp_core")


def shifted(block, axis, distance):
    devices = range(lax.axis_size(axis))
    route = [(i - distance, i) for i in devices if i - distance in devices]
    return lax.ppermute(block, axis, route)


def rotated(block, axis, shift):
    n = lax.axis_size(axis)
    return lax.ppermute(block, axis, [(i, (i + shift) % n) for i in range(n)])


def swapped(block, axis):
    return lax.ppermute(block, axis, [(0, 1), (1, 0)])


def head_forward(queries, key_rows, values):
    score_scale = queries.shape[-1] ** (-0.5)
    scores = jnp.dot(queries, key_rows.T, preferred_element_type=jnp.float32) * score_scale
    row_ids = lax.broadcasted_iota(jnp.int32, scores.shape, 0)
    col_ids = lax.broadcasted_iota(jnp.int32, scores.shape, 1)
    scores = jnp.where(col_ids <= row_ids, scores, -1e30)
    row_max = jnp.max(scores, axis=1, keepdims=True)
    weights = jnp.exp(scores - row_max)
    softmax = weights / jnp.sum(weights, axis=1, keepdims=True)
    soft_low = softmax.astype(jnp.bfloat16)
    attended = jnp.dot(soft_low, values, preferred_element_type=jnp.float32).astype(jnp.bfloat16)
    return (softmax, soft_low, attended)


def head_backward(queries, key_rows, values, softmax, soft_low, attended, grad_head):
    score_scale = queries.shape[-1] ** (-0.5)
    row_dot = jnp.sum(
        grad_head.astype(jnp.float32) * attended.astype(jnp.float32), axis=1, keepdims=True
    )
    grad_values = jnp.dot(soft_low.T, grad_head, preferred_element_type=jnp.float32)
    grad_probs = jnp.dot(grad_head, values.T, preferred_element_type=jnp.float32)
    grad_scores = (softmax * (grad_probs - row_dot)).astype(jnp.bfloat16)
    grad_query = jnp.dot(grad_scores, key_rows, preferred_element_type=jnp.float32) * score_scale
    grad_keys = jnp.dot(grad_scores.T, queries, preferred_element_type=jnp.float32) * score_scale
    return jnp.concatenate([grad_query, grad_keys, grad_values], axis=1).astype(jnp.bfloat16)


def weight_grad_sum(weight_part):
    n_y, n_z, n_core = (lax.axis_size(a) for a in DP_PARTS)
    rows = weight_part.shape[0] // (n_y * n_z * n_core)
    blocks = weight_part.reshape(n_y, n_z, n_core, rows, weight_part.shape[1])
    core = lax.axis_index("dp_core")
    keep = lax.dynamic_index_in_dim(blocks, core, axis=2, keepdims=False)
    give = lax.dynamic_index_in_dim(blocks, 1 - core, axis=2, keepdims=False)
    pair = keep + swapped(give, "dp_core")
    y = lax.axis_index("dp_y")
    keep = lax.dynamic_index_in_dim(pair, y, axis=0, keepdims=False)
    give = lax.dynamic_index_in_dim(pair, 1 - y, axis=0, keepdims=False)
    quad = keep + swapped(give.astype(jnp.bfloat16), "dp_y").astype(jnp.float32)
    z = lax.axis_index("dp_z")
    low = quad.astype(jnp.bfloat16)
    ring = lax.dynamic_slice_in_dim(jnp.concatenate([low, low], axis=0), z, n_z, axis=0)
    total = lax.dynamic_index_in_dim(quad, z, axis=0, keepdims=False)
    for shift in range(1, n_z):
        total = total + rotated(ring[shift], "dp_z", shift).astype(jnp.float32)
    return total


def input_grad_sum(partials):
    n = partials.shape[0]
    total = partials[0].astype(jnp.float32)
    for shift in range(1, n):
        total = total + rotated(partials[shift], "tensor", shift).astype(jnp.float32)
    return total


def body(grad_out, qkv_saved, w_out, w_qkv, plan):
    gradients = grad_out[0, :, 0]
    saved_qkv = qkv_saved[0, :, 0, :, 0]
    out_proj = w_out[0, :, 0]
    qkv_proj = w_qkv[0, :, 0]
    head_size = out_proj.shape[1]
    seq_len = gradients.shape[1]
    queries = saved_qkv[:, :, :head_size]
    key_rows = saved_qkv[:, :, head_size : 2 * head_size]
    values = saved_qkv[:, :, 2 * head_size :]
    softmax, soft_low, attended = jax.vmap(head_forward)(queries, key_rows, values)
    weight_part = jnp.einsum("msc,msh->ch", gradients, attended, preferred_element_type=jnp.float32)
    weight_grad = weight_grad_sum(weight_part)
    current = plan[0, :BMICRO]
    grad_heads = jnp.einsum(
        "msd,dh->msh", gradients, out_proj, preferred_element_type=jnp.float32
    ).astype(jnp.bfloat16)
    grad_qkv = jax.vmap(head_backward)(
        jnp.take(queries, current, axis=0),
        jnp.take(key_rows, current, axis=0),
        jnp.take(values, current, axis=0),
        jnp.take(softmax, current, axis=0),
        jnp.take(soft_low, current, axis=0),
        jnp.take(attended, current, axis=0),
        jnp.take(grad_heads, current, axis=0),
    )
    n_tensor = lax.axis_size("tensor")
    share_rows = seq_len // n_tensor
    start = lax.axis_index("tensor") * share_rows
    grad_qkv = lax.dynamic_slice_in_dim(jnp.concatenate([grad_qkv, grad_qkv], axis=1), start, seq_len, axis=1)
    partials = jnp.einsum("bsk,dk->sbd", grad_qkv, qkv_proj, preferred_element_type=jnp.float32)
    partials = partials.astype(jnp.bfloat16).reshape(n_tensor, share_rows, *partials.shape[1:])
    own_rows = input_grad_sum(partials)
    received = shifted(own_rows.astype(jnp.bfloat16), "pipe", -1)
    return (received[None, None], weight_grad[None, :, None, :])


def solution(mesh):
    n_pipe, n_dp, n_tensor = (mesh.shape[a] for a in ("pipe", "dp", "tensor"))
    n_y = 2
    n_core = 2
    parts = mesh.devices.reshape(n_pipe, n_y, n_dp // (n_y * n_core), n_core, n_tensor)
    staged = Mesh(parts, ("pipe", *DP_PARTS, "tensor"))
    in_specs = (
        P("pipe", None, DP_PARTS, None, None),
        P("pipe", None, DP_PARTS, None, "tensor", None),
        P("pipe", None, "tensor", None),
        P("pipe", None, "tensor", None),
        P("pipe", None),
    )
    out_specs = (P("pipe", DP_PARTS, "tensor", None, None), P("pipe", DP_PARTS, "tensor", None))
    return jax.shard_map(body, mesh=staged, in_specs=in_specs, out_specs=out_specs, check_vma=False)
```

```python
import jax
import jax.numpy as jnp
from jax import lax
from jax.sharding import Mesh, PartitionSpec as P

BMICRO = 2
DP_PARTS = ("dp_y", "dp_z", "dp_core")
DP_FAR = ("dp_y", "dp_z")


def shifted(block, axis, distance):
    devices = range(lax.axis_size(axis))
    route = [(i - distance, i) for i in devices if i - distance in devices]
    return lax.ppermute(block, axis, route)


def exchange(block, axis):
    n = lax.axis_size(axis)
    parts = block.reshape(n, block.shape[0] // n, *block.shape[1:])
    return lax.all_to_all(parts, axis, 0, 0, tiled=True)


def ordered_sum(parts):
    total = parts[0].astype(jnp.float32)
    for index in range(1, parts.shape[0]):
        total = total + parts[index].astype(jnp.float32)
    return total


def weight_grad_sum(weight_part):
    n_far = lax.axis_size(DP_FAR)
    n_core = lax.axis_size("dp_core")
    rows = weight_part.shape[0] // (n_far * n_core)
    blocks = weight_part.reshape(n_far, n_core, rows, weight_part.shape[1])
    pair = lax.all_to_all(blocks, "dp_core", 1, 1, tiled=True)
    pair = pair[:, 0] + pair[:, 1]
    return jnp.sum(lax.all_to_all(pair.astype(jnp.bfloat16), DP_FAR, 0, 0, tiled=True).astype(jnp.float32), axis=0)


def head_forward(queries, key_rows, values):
    score_scale = queries.shape[-1] ** (-0.5)
    scores = jnp.dot(queries, key_rows.T, preferred_element_type=jnp.float32) * score_scale
    row_ids = lax.broadcasted_iota(jnp.int32, scores.shape, 0)
    col_ids = lax.broadcasted_iota(jnp.int32, scores.shape, 1)
    scores = jnp.where(col_ids <= row_ids, scores, -1e30)
    row_max = jnp.max(scores, axis=1, keepdims=True)
    weights = jnp.exp(scores - row_max)
    softmax = weights / jnp.sum(weights, axis=1, keepdims=True)
    soft_low = softmax.astype(jnp.bfloat16)
    attended = jnp.dot(soft_low, values, preferred_element_type=jnp.float32).astype(jnp.bfloat16)
    return (softmax, soft_low, attended)


def head_backward(queries, key_rows, values, softmax, soft_low, attended, grad_head):
    score_scale = queries.shape[-1] ** (-0.5)
    row_dot = jnp.sum(
        grad_head.astype(jnp.float32) * attended.astype(jnp.float32), axis=1, keepdims=True
    )
    grad_values = jnp.dot(soft_low.T, grad_head, preferred_element_type=jnp.float32)
    grad_probs = jnp.dot(grad_head, values.T, preferred_element_type=jnp.float32)
    grad_scores = (softmax * (grad_probs - row_dot)).astype(jnp.bfloat16)
    grad_query = jnp.dot(grad_scores, key_rows, preferred_element_type=jnp.float32) * score_scale
    grad_keys = jnp.dot(grad_scores.T, queries, preferred_element_type=jnp.float32) * score_scale
    return jnp.concatenate([grad_query, grad_keys, grad_values], axis=1).astype(jnp.bfloat16)


def body(grad_out, qkv_saved, w_out, w_qkv, plan):
    gradients = grad_out[0, :, 0]
    saved_qkv = qkv_saved[0, :, 0, :, 0]
    out_proj = w_out[0, :, 0]
    qkv_proj = w_qkv[0, :, 0]
    head_size = out_proj.shape[1]
    queries = saved_qkv[:, :, :head_size]
    key_rows = saved_qkv[:, :, head_size : 2 * head_size]
    values = saved_qkv[:, :, 2 * head_size :]
    softmax, soft_low, attended = jax.vmap(head_forward)(queries, key_rows, values)
    weight_part = jnp.einsum("msc,msh->ch", gradients, attended, preferred_element_type=jnp.float32)
    weight_grad = weight_grad_sum(weight_part)
    current = plan[0, :BMICRO]
    grad_heads = jnp.einsum(
        "msd,dh->msh", gradients, out_proj, preferred_element_type=jnp.float32
    ).astype(jnp.bfloat16)
    grad_qkv = jax.vmap(head_backward)(
        jnp.take(queries, current, axis=0),
        jnp.take(key_rows, current, axis=0),
        jnp.take(values, current, axis=0),
        jnp.take(softmax, current, axis=0),
        jnp.take(soft_low, current, axis=0),
        jnp.take(attended, current, axis=0),
        jnp.take(grad_heads, current, axis=0),
    )
    n_tensor = lax.axis_size("tensor")
    grouped = grad_qkv.reshape(grad_qkv.shape[0], n_tensor, grad_qkv.shape[1] // n_tensor, grad_qkv.shape[2])
    partials = jnp.einsum("bjsk,dk->jsbd", grouped, qkv_proj, preferred_element_type=jnp.float32)
    parts = lax.all_to_all(partials.astype(jnp.bfloat16), "tensor", 0, 0, tiled=True)
    own_rows = ordered_sum(parts)
    received = shifted(own_rows.astype(jnp.bfloat16), "pipe", -1)
    return (received[None, None], weight_grad[None, :, None, :])


def solution(mesh):
    n_pipe, n_dp, n_tensor = (mesh.shape[a] for a in ("pipe", "dp", "tensor"))
    n_y = 2
    n_core = 2
    parts = mesh.devices.reshape(n_pipe, n_y, n_dp // (n_y * n_core), n_core, n_tensor)
    staged = Mesh(parts, ("pipe", *DP_PARTS, "tensor"))
    in_specs = (
        P("pipe", None, DP_PARTS, None, None),
        P("pipe", None, DP_PARTS, None, "tensor", None),
        P("pipe", None, "tensor", None),
        P("pipe", None, "tensor", None),
        P("pipe", None),
    )
    out_specs = (P("pipe", DP_PARTS, "tensor", None, None), P("pipe", DP_PARTS, "tensor", None))
    return jax.shard_map(body, mesh=staged, in_specs=in_specs, out_specs=out_specs, check_vma=False)
```

```python
import jax
import jax.numpy as jnp
from jax import lax
from jax.sharding import Mesh, PartitionSpec as P

BMICRO = 2
DP_PARTS = ("dp_y", "dp_z", "dp_core")
DP_FAR = ("dp_y", "dp_z")


def shifted(block, axis, distance):
    devices = range(lax.axis_size(axis))
    route = [(i - distance, i) for i in devices if i - distance in devices]
    return lax.ppermute(block, axis, route)


def exchange(block, axis):
    n = lax.axis_size(axis)
    parts = block.reshape(n, block.shape[0] // n, *block.shape[1:])
    return lax.all_to_all(parts, axis, 0, 0, tiled=True)


def ordered_sum(parts):
    total = parts[0].astype(jnp.float32)
    for index in range(1, parts.shape[0]):
        total = total + parts[index].astype(jnp.float32)
    return total


def weight_grad_sum(weight_part):
    pair = lax.all_to_all(weight_part, "dp_core", 2, 2, tiled=True)
    pair = (pair[:, :, 0] + pair[:, :, 1]).astype(jnp.bfloat16)
    return jnp.sum(lax.all_to_all(pair, DP_FAR, 1, 1, tiled=True).astype(jnp.float32), axis=1).T


def head_forward(queries, key_rows, values):
    score_scale = queries.shape[-1] ** (-0.5)
    scores = jnp.dot(queries, key_rows.T, preferred_element_type=jnp.float32) * score_scale
    row_ids = lax.broadcasted_iota(jnp.int32, scores.shape, 0)
    col_ids = lax.broadcasted_iota(jnp.int32, scores.shape, 1)
    scores = jnp.where(col_ids <= row_ids, scores, -1e30)
    row_max = jnp.max(scores, axis=1, keepdims=True)
    weights = jnp.exp(scores - row_max)
    softmax = weights / jnp.sum(weights, axis=1, keepdims=True)
    soft_low = softmax.astype(jnp.bfloat16)
    attended = jnp.dot(soft_low, values, preferred_element_type=jnp.float32).astype(jnp.bfloat16)
    return (softmax, soft_low, attended)


def head_backward(queries, key_rows, values, softmax, soft_low, attended, grad_head):
    score_scale = queries.shape[-1] ** (-0.5)
    row_dot = jnp.sum(
        grad_head.astype(jnp.float32) * attended.astype(jnp.float32), axis=1, keepdims=True
    )
    grad_values = jnp.dot(soft_low.T, grad_head, preferred_element_type=jnp.float32)
    grad_probs = jnp.dot(grad_head, values.T, preferred_element_type=jnp.float32)
    grad_scores = (softmax * (grad_probs - row_dot)).astype(jnp.bfloat16)
    grad_query = jnp.dot(grad_scores, key_rows, preferred_element_type=jnp.float32) * score_scale
    grad_keys = jnp.dot(grad_scores.T, queries, preferred_element_type=jnp.float32) * score_scale
    return jnp.concatenate([grad_query, grad_keys, grad_values], axis=1).astype(jnp.bfloat16)


def body(grad_out, qkv_saved, w_out, w_qkv, plan):
    gradients = grad_out[0, :, 0]
    saved_qkv = qkv_saved[0, :, 0, :, 0]
    out_proj = w_out[0, :, 0]
    qkv_proj = w_qkv[0, :, 0]
    head_size = out_proj.shape[1]
    queries = saved_qkv[:, :, :head_size]
    key_rows = saved_qkv[:, :, head_size : 2 * head_size]
    values = saved_qkv[:, :, 2 * head_size :]
    softmax, soft_low, attended = jax.vmap(head_forward)(queries, key_rows, values)
    n_far = lax.axis_size(DP_FAR)
    n_core = lax.axis_size("dp_core")
    weight_part = jnp.einsum("msc,msh->hc", gradients, attended, preferred_element_type=jnp.float32)
    weight_part = weight_part.reshape(weight_part.shape[0], n_far, n_core, -1)
    weight_grad = weight_grad_sum(weight_part)
    current = plan[0, :BMICRO]
    grad_heads = jnp.einsum(
        "msd,dh->msh", gradients, out_proj, preferred_element_type=jnp.float32
    ).astype(jnp.bfloat16)
    grad_qkv = jax.vmap(head_backward)(
        jnp.take(queries, current, axis=0),
        jnp.take(key_rows, current, axis=0),
        jnp.take(values, current, axis=0),
        jnp.take(softmax, current, axis=0),
        jnp.take(soft_low, current, axis=0),
        jnp.take(attended, current, axis=0),
        jnp.take(grad_heads, current, axis=0),
    )
    n_tensor = lax.axis_size("tensor")
    grouped = grad_qkv.reshape(grad_qkv.shape[0], n_tensor, grad_qkv.shape[1] // n_tensor, grad_qkv.shape[2])
    partials = jnp.einsum("bjsk,dk->jsbd", grouped, qkv_proj, preferred_element_type=jnp.float32)
    parts = lax.all_to_all(partials.astype(jnp.bfloat16), "tensor", 0, 0, tiled=True)
    own_rows = ordered_sum(parts)
    received = shifted(own_rows.astype(jnp.bfloat16), "pipe", -1)
    return (received[None, None], weight_grad[None, :, None, :])


def solution(mesh):
    n_pipe, n_dp, n_tensor = (mesh.shape[a] for a in ("pipe", "dp", "tensor"))
    n_y = 2
    n_core = 2
    parts = mesh.devices.reshape(n_pipe, n_y, n_dp // (n_y * n_core), n_core, n_tensor)
    staged = Mesh(parts, ("pipe", *DP_PARTS, "tensor"))
    in_specs = (
        P("pipe", None, DP_PARTS, None, None),
        P("pipe", None, DP_PARTS, None, "tensor", None),
        P("pipe", None, "tensor", None),
        P("pipe", None, "tensor", None),
        P("pipe", None),
    )
    out_specs = (P("pipe", DP_PARTS, "tensor", None, None), P("pipe", DP_PARTS, "tensor", None))
    return jax.shard_map(body, mesh=staged, in_specs=in_specs, out_specs=out_specs, check_vma=False)
```

```python
import jax
import jax.numpy as jnp
from jax import lax
from jax.sharding import Mesh, PartitionSpec as P

BMICRO = 2
DP_PARTS = ("dp_y", "dp_z", "dp_core")
DP_FAR = ("dp_y", "dp_z")


def shifted(block, axis, distance):
    devices = range(lax.axis_size(axis))
    route = [(i - distance, i) for i in devices if i - distance in devices]
    return lax.ppermute(block, axis, route)


def exchange(block, axis):
    n = lax.axis_size(axis)
    parts = block.reshape(n, block.shape[0] // n, *block.shape[1:])
    return lax.all_to_all(parts, axis, 0, 0, tiled=True)


def ordered_sum(parts):
    total = parts[0].astype(jnp.float32)
    for index in range(1, parts.shape[0]):
        total = total + parts[index].astype(jnp.float32)
    return total


def rotated_sum(parts, axis):
    n = parts.shape[0]
    total = parts[0].astype(jnp.float32)
    for shift in range(1, n):
        moved = lax.ppermute(parts[shift], axis, [(i, (i + shift) % n) for i in range(n)])
        total = total + moved.astype(jnp.float32)
    return total


def weight_grad_sum(weight_part):
    pair = lax.all_to_all(weight_part, "dp_core", 2, 2, tiled=True)
    pair = (pair[:, :, 0] + pair[:, :, 1]).astype(jnp.bfloat16)
    return jnp.sum(lax.all_to_all(pair, DP_FAR, 1, 1, tiled=True).astype(jnp.float32), axis=1).T


def head_forward(queries, key_rows, values):
    score_scale = queries.shape[-1] ** (-0.5)
    scores = jnp.dot(queries, key_rows.T, preferred_element_type=jnp.float32) * score_scale
    row_ids = lax.broadcasted_iota(jnp.int32, scores.shape, 0)
    col_ids = lax.broadcasted_iota(jnp.int32, scores.shape, 1)
    scores = jnp.where(col_ids <= row_ids, scores, -1e30)
    row_max = jnp.max(scores, axis=1, keepdims=True)
    weights = jnp.exp(scores - row_max)
    softmax = weights / jnp.sum(weights, axis=1, keepdims=True)
    soft_low = softmax.astype(jnp.bfloat16)
    attended = jnp.dot(soft_low, values, preferred_element_type=jnp.float32).astype(jnp.bfloat16)
    return (softmax, soft_low, attended)


def head_backward(queries, key_rows, values, softmax, soft_low, attended, grad_head):
    score_scale = queries.shape[-1] ** (-0.5)
    row_dot = jnp.sum(
        grad_head.astype(jnp.float32) * attended.astype(jnp.float32), axis=1, keepdims=True
    )
    grad_values = jnp.dot(soft_low.T, grad_head, preferred_element_type=jnp.float32)
    grad_probs = jnp.dot(grad_head, values.T, preferred_element_type=jnp.float32)
    grad_scores = (softmax * (grad_probs - row_dot)).astype(jnp.bfloat16)
    grad_query = jnp.dot(grad_scores, key_rows, preferred_element_type=jnp.float32) * score_scale
    grad_keys = jnp.dot(grad_scores.T, queries, preferred_element_type=jnp.float32) * score_scale
    return jnp.concatenate([grad_query, grad_keys, grad_values], axis=1).astype(jnp.bfloat16)


def body(grad_out, qkv_saved, w_out, w_qkv, plan):
    gradients = grad_out[0, :, 0]
    saved_qkv = qkv_saved[0, :, 0, :, 0]
    out_proj = w_out[0, :, 0]
    qkv_proj = w_qkv[0, :, 0]
    head_size = out_proj.shape[1]
    queries = saved_qkv[:, :, :head_size]
    key_rows = saved_qkv[:, :, head_size : 2 * head_size]
    values = saved_qkv[:, :, 2 * head_size :]
    softmax, soft_low, attended = jax.vmap(head_forward)(queries, key_rows, values)
    n_far = lax.axis_size(DP_FAR)
    n_core = lax.axis_size("dp_core")
    weight_part = jnp.einsum("msc,msh->hc", gradients, attended, preferred_element_type=jnp.float32)
    weight_part = weight_part.reshape(weight_part.shape[0], n_far, n_core, -1)
    weight_grad = weight_grad_sum(weight_part)
    current = plan[0, :BMICRO]
    grad_heads = jnp.einsum(
        "msd,dh->msh", gradients, out_proj, preferred_element_type=jnp.float32
    ).astype(jnp.bfloat16)
    grad_qkv = jax.vmap(head_backward)(
        jnp.take(queries, current, axis=0),
        jnp.take(key_rows, current, axis=0),
        jnp.take(values, current, axis=0),
        jnp.take(softmax, current, axis=0),
        jnp.take(soft_low, current, axis=0),
        jnp.take(attended, current, axis=0),
        jnp.take(grad_heads, current, axis=0),
    )
    n_tensor = lax.axis_size("tensor")
    seq_len = grad_qkv.shape[1]
    start = lax.axis_index("tensor") * (seq_len // n_tensor)
    grad_qkv = lax.dynamic_slice_in_dim(jnp.concatenate([grad_qkv, grad_qkv], axis=1), start, seq_len, axis=1)
    grouped = grad_qkv.reshape(grad_qkv.shape[0], n_tensor, seq_len // n_tensor, grad_qkv.shape[2])
    partials = jnp.einsum("bjsk,dk->jsbd", grouped, qkv_proj, preferred_element_type=jnp.float32)
    own_rows = rotated_sum(partials.astype(jnp.bfloat16), "tensor")
    received = shifted(own_rows.astype(jnp.bfloat16), "pipe", -1)
    return (received[None, None], weight_grad[None, :, None, :])


def solution(mesh):
    n_pipe, n_dp, n_tensor = (mesh.shape[a] for a in ("pipe", "dp", "tensor"))
    n_y = 2
    n_core = 2
    parts = mesh.devices.reshape(n_pipe, n_y, n_dp // (n_y * n_core), n_core, n_tensor)
    staged = Mesh(parts, ("pipe", *DP_PARTS, "tensor"))
    in_specs = (
        P("pipe", None, DP_PARTS, None, None),
        P("pipe", None, DP_PARTS, None, "tensor", None),
        P("pipe", None, "tensor", None),
        P("pipe", None, "tensor", None),
        P("pipe", None),
    )
    out_specs = (P("pipe", DP_PARTS, "tensor", None, None), P("pipe", DP_PARTS, "tensor", None))
    return jax.shard_map(body, mesh=staged, in_specs=in_specs, out_specs=out_specs, check_vma=False)
```

```python
import jax
import jax.numpy as jnp
from jax import lax
from jax.sharding import Mesh, PartitionSpec as P

BMICRO = 2
DP_PARTS = ("dp_y", "dp_z", "dp_core")


def shifted(block, axis, distance):
    devices = range(lax.axis_size(axis))
    route = [(i - distance, i) for i in devices if i - distance in devices]
    return lax.ppermute(block, axis, route)


def exchange(block, axis):
    n = lax.axis_size(axis)
    parts = block.reshape(n, block.shape[0] // n, *block.shape[1:])
    return lax.all_to_all(parts, axis, 0, 0, tiled=True)


def ordered_sum(parts):
    total = parts[0].astype(jnp.float32)
    for index in range(1, parts.shape[0]):
        total = total + parts[index].astype(jnp.float32)
    return total


def rotated_sum(parts, axis):
    n = parts.shape[0]
    total = parts[0].astype(jnp.float32)
    for shift in range(1, n):
        moved = lax.ppermute(parts[shift], axis, [(i, (i + shift) % n) for i in range(n)])
        total = total + moved.astype(jnp.float32)
    return total


def weight_grad_sum(weight_part):
    pair = lax.all_to_all(weight_part, "dp_core", 3, 3, tiled=True)
    pair = (pair[:, :, :, 0] + pair[:, :, :, 1]).astype(jnp.bfloat16)
    ring = jnp.sum(lax.all_to_all(pair, "dp_z", 2, 2, tiled=True).astype(jnp.float32), axis=2)
    y = lax.axis_index("dp_y")
    keep = lax.dynamic_index_in_dim(ring, y, axis=1, keepdims=False)
    give = lax.dynamic_index_in_dim(ring, 1 - y, axis=1, keepdims=False)
    return (keep + lax.ppermute(give, "dp_y", [(0, 1), (1, 0)])).T


def head_forward(queries, key_rows, values):
    score_scale = queries.shape[-1] ** (-0.5)
    scores = jnp.dot(queries, key_rows.T, preferred_element_type=jnp.float32) * score_scale
    row_ids = lax.broadcasted_iota(jnp.int32, scores.shape, 0)
    col_ids = lax.broadcasted_iota(jnp.int32, scores.shape, 1)
    scores = jnp.where(col_ids <= row_ids, scores, -1e30)
    row_max = jnp.max(scores, axis=1, keepdims=True)
    weights = jnp.exp(scores - row_max)
    softmax = weights / jnp.sum(weights, axis=1, keepdims=True)
    soft_low = softmax.astype(jnp.bfloat16)
    attended = jnp.dot(soft_low, values, preferred_element_type=jnp.float32).astype(jnp.bfloat16)
    return (softmax, soft_low, attended)


def head_backward(queries, key_rows, values, softmax, soft_low, attended, grad_head):
    score_scale = queries.shape[-1] ** (-0.5)
    row_dot = jnp.sum(
        grad_head.astype(jnp.float32) * attended.astype(jnp.float32), axis=1, keepdims=True
    )
    grad_values = jnp.dot(soft_low.T, grad_head, preferred_element_type=jnp.float32)
    grad_probs = jnp.dot(grad_head, values.T, preferred_element_type=jnp.float32)
    grad_scores = (softmax * (grad_probs - row_dot)).astype(jnp.bfloat16)
    grad_query = jnp.dot(grad_scores, key_rows, preferred_element_type=jnp.float32) * score_scale
    grad_keys = jnp.dot(grad_scores.T, queries, preferred_element_type=jnp.float32) * score_scale
    return jnp.concatenate([grad_query, grad_keys, grad_values], axis=1).astype(jnp.bfloat16)


def body(grad_out, qkv_saved, w_out, w_qkv, plan):
    gradients = grad_out[0, :, 0]
    saved_qkv = qkv_saved[0, :, 0, :, 0]
    out_proj = w_out[0, :, 0]
    qkv_proj = w_qkv[0, :, 0]
    head_size = out_proj.shape[1]
    queries = saved_qkv[:, :, :head_size]
    key_rows = saved_qkv[:, :, head_size : 2 * head_size]
    values = saved_qkv[:, :, 2 * head_size :]
    softmax, soft_low, attended = jax.vmap(head_forward)(queries, key_rows, values)
    weight_part = jnp.einsum("msc,msh->hc", gradients, attended, preferred_element_type=jnp.float32)
    weight_part = weight_part.reshape(weight_part.shape[0], *(lax.axis_size(a) for a in DP_PARTS), -1)
    weight_grad = weight_grad_sum(weight_part)
    current = plan[0, :BMICRO]
    grad_heads = jnp.einsum(
        "msd,dh->msh", gradients, out_proj, preferred_element_type=jnp.float32
    ).astype(jnp.bfloat16)
    grad_qkv = jax.vmap(head_backward)(
        jnp.take(queries, current, axis=0),
        jnp.take(key_rows, current, axis=0),
        jnp.take(values, current, axis=0),
        jnp.take(softmax, current, axis=0),
        jnp.take(soft_low, current, axis=0),
        jnp.take(attended, current, axis=0),
        jnp.take(grad_heads, current, axis=0),
    )
    n_tensor = lax.axis_size("tensor")
    seq_len = grad_qkv.shape[1]
    start = lax.axis_index("tensor") * (seq_len // n_tensor)
    grad_qkv = lax.dynamic_slice_in_dim(jnp.concatenate([grad_qkv, grad_qkv], axis=1), start, seq_len, axis=1)
    grouped = grad_qkv.reshape(grad_qkv.shape[0], n_tensor, seq_len // n_tensor, grad_qkv.shape[2])
    partials = jnp.einsum("bjsk,dk->jsbd", grouped, qkv_proj, preferred_element_type=jnp.float32)
    own_rows = rotated_sum(partials.astype(jnp.bfloat16), "tensor")
    received = shifted(own_rows.astype(jnp.bfloat16), "pipe", -1)
    return (received[None, None], weight_grad[None, :, None, :])


def solution(mesh):
    n_pipe, n_dp, n_tensor = (mesh.shape[a] for a in ("pipe", "dp", "tensor"))
    n_y = 2
    n_core = 2
    parts = mesh.devices.reshape(n_pipe, n_y, n_dp // (n_y * n_core), n_core, n_tensor)
    staged = Mesh(parts, ("pipe", *DP_PARTS, "tensor"))
    in_specs = (
        P("pipe", None, DP_PARTS, None, None),
        P("pipe", None, DP_PARTS, None, "tensor", None),
        P("pipe", None, "tensor", None),
        P("pipe", None, "tensor", None),
        P("pipe", None),
    )
    out_specs = (P("pipe", DP_PARTS, "tensor", None, None), P("pipe", DP_PARTS, "tensor", None))
    return jax.shard_map(body, mesh=staged, in_specs=in_specs, out_specs=out_specs, check_vma=False)
```

```python
import jax
import jax.numpy as jnp
from jax import lax
from jax.experimental.layout import Layout, with_layout_constraint
from jax.sharding import Mesh, PartitionSpec as P

BMICRO = 2
DP_PARTS = ("dp_y", "dp_z", "dp_core")
DP_FAR = ("dp_y", "dp_z")


def shifted(block, axis, distance):
    devices = range(lax.axis_size(axis))
    route = [(i - distance, i) for i in devices if i - distance in devices]
    return lax.ppermute(block, axis, route)


def exchange(block, axis):
    n = lax.axis_size(axis)
    parts = block.reshape(n, block.shape[0] // n, *block.shape[1:])
    return lax.all_to_all(parts, axis, 0, 0, tiled=True)


def ordered_sum(parts):
    total = parts[0].astype(jnp.float32)
    for index in range(1, parts.shape[0]):
        total = total + parts[index].astype(jnp.float32)
    return total


def rotated_sum(parts, axis):
    n = parts.shape[0]
    total = parts[0].astype(jnp.float32)
    for shift in range(1, n):
        moved = lax.ppermute(parts[shift], axis, [(i, (i + shift) % n) for i in range(n)])
        total = total + moved.astype(jnp.float32)
    return total


def weight_grad_sum(weight_part):
    n_far = lax.axis_size(DP_FAR)
    n_core = lax.axis_size("dp_core")
    blocks = weight_part.reshape(n_far, n_core, weight_part.shape[0] // (n_far * n_core), weight_part.shape[1])
    pair = lax.all_to_all(blocks, "dp_core", 1, 1, tiled=True)
    pair = (pair[:, 0].astype(jnp.float32) + pair[:, 1].astype(jnp.float32)).astype(jnp.bfloat16)
    return jnp.sum(lax.all_to_all(pair, DP_FAR, 0, 0, tiled=True).astype(jnp.float32), axis=0)


def head_forward(queries, key_rows, values):
    score_scale = queries.shape[-1] ** (-0.5)
    scores = jnp.dot(queries, key_rows.T, preferred_element_type=jnp.float32) * score_scale
    row_ids = lax.broadcasted_iota(jnp.int32, scores.shape, 0)
    col_ids = lax.broadcasted_iota(jnp.int32, scores.shape, 1)
    scores = jnp.where(col_ids <= row_ids, scores, -1e30)
    row_max = jnp.max(scores, axis=1, keepdims=True)
    weights = jnp.exp(scores - row_max)
    softmax = weights / jnp.sum(weights, axis=1, keepdims=True)
    soft_low = softmax.astype(jnp.bfloat16)
    attended = jnp.dot(soft_low, values, preferred_element_type=jnp.float32).astype(jnp.bfloat16)
    return (softmax, soft_low, attended)


def head_backward(queries, key_rows, values, softmax, soft_low, attended, grad_head):
    score_scale = queries.shape[-1] ** (-0.5)
    row_dot = jnp.sum(
        grad_head.astype(jnp.float32) * attended.astype(jnp.float32), axis=1, keepdims=True
    )
    grad_values = jnp.dot(soft_low.T, grad_head, preferred_element_type=jnp.float32)
    grad_probs = jnp.dot(grad_head, values.T, preferred_element_type=jnp.float32)
    grad_scores = (softmax * (grad_probs - row_dot)).astype(jnp.bfloat16)
    grad_query = jnp.dot(grad_scores, key_rows, preferred_element_type=jnp.float32) * score_scale
    grad_keys = jnp.dot(grad_scores.T, queries, preferred_element_type=jnp.float32) * score_scale
    return jnp.concatenate([grad_query, grad_keys, grad_values], axis=1).astype(jnp.bfloat16)


def body(grad_out, qkv_saved, w_out, w_qkv, plan):
    gradients = grad_out[0, :, 0]
    saved_qkv = qkv_saved[0, :, 0, :, 0]
    out_proj = w_out[0, :, 0]
    qkv_proj = w_qkv[0, :, 0]
    head_size = out_proj.shape[1]
    queries = saved_qkv[:, :, :head_size]
    key_rows = saved_qkv[:, :, head_size : 2 * head_size]
    values = saved_qkv[:, :, 2 * head_size :]
    softmax, soft_low, attended = jax.vmap(head_forward)(queries, key_rows, values)
    weight_part = jnp.einsum("msc,msh->ch", gradients, attended, preferred_element_type=jnp.float32)
    weight_part = with_layout_constraint(weight_part.astype(jnp.bfloat16), Layout((0, 1)))
    weight_grad = weight_grad_sum(weight_part)
    current = plan[0, :BMICRO]
    grad_heads = jnp.einsum(
        "msd,dh->msh", gradients, out_proj, preferred_element_type=jnp.float32
    ).astype(jnp.bfloat16)
    grad_qkv = jax.vmap(head_backward)(
        jnp.take(queries, current, axis=0),
        jnp.take(key_rows, current, axis=0),
        jnp.take(values, current, axis=0),
        jnp.take(softmax, current, axis=0),
        jnp.take(soft_low, current, axis=0),
        jnp.take(attended, current, axis=0),
        jnp.take(grad_heads, current, axis=0),
    )
    n_tensor = lax.axis_size("tensor")
    seq_len = grad_qkv.shape[1]
    start = lax.axis_index("tensor") * (seq_len // n_tensor)
    grad_qkv = lax.dynamic_slice_in_dim(jnp.concatenate([grad_qkv, grad_qkv], axis=1), start, seq_len, axis=1)
    grouped = grad_qkv.reshape(grad_qkv.shape[0], n_tensor, seq_len // n_tensor, grad_qkv.shape[2])
    partials = jnp.einsum("bjsk,dk->jsbd", grouped, qkv_proj, preferred_element_type=jnp.float32)
    own_rows = rotated_sum(partials.astype(jnp.bfloat16), "tensor")
    received = shifted(own_rows.astype(jnp.bfloat16), "pipe", -1)
    return (received[None, None], weight_grad[None, :, None, :])


def solution(mesh):
    n_pipe, n_dp, n_tensor = (mesh.shape[a] for a in ("pipe", "dp", "tensor"))
    n_y = 2
    n_core = 2
    parts = mesh.devices.reshape(n_pipe, n_y, n_dp // (n_y * n_core), n_core, n_tensor)
    staged = Mesh(parts, ("pipe", *DP_PARTS, "tensor"))
    in_specs = (
        P("pipe", None, DP_PARTS, None, None),
        P("pipe", None, DP_PARTS, None, "tensor", None),
        P("pipe", None, "tensor", None),
        P("pipe", None, "tensor", None),
        P("pipe", None),
    )
    out_specs = (P("pipe", DP_PARTS, "tensor", None, None), P("pipe", DP_PARTS, "tensor", None))
    return jax.shard_map(body, mesh=staged, in_specs=in_specs, out_specs=out_specs, check_vma=False)
```

```python
import jax
import jax.numpy as jnp
from jax import lax
from jax.experimental.layout import Layout, with_layout_constraint
from jax.sharding import Mesh, PartitionSpec as P

BMICRO = 2
DP_PARTS = ("dp_y", "dp_z", "dp_core")
DP_FAR = ("dp_y", "dp_z")


def shifted(block, axis, distance):
    devices = range(lax.axis_size(axis))
    route = [(i - distance, i) for i in devices if i - distance in devices]
    return lax.ppermute(block, axis, route)


def exchange(block, axis):
    n = lax.axis_size(axis)
    parts = block.reshape(n, block.shape[0] // n, *block.shape[1:])
    return lax.all_to_all(parts, axis, 0, 0, tiled=True)


def ordered_sum(parts):
    total = parts[0].astype(jnp.float32)
    for index in range(1, parts.shape[0]):
        total = total + parts[index].astype(jnp.float32)
    return total


def rotated_sum(parts, axis):
    n = parts.shape[0]
    total = parts[0].astype(jnp.float32)
    for shift in range(1, n):
        moved = lax.ppermute(parts[shift], axis, [(i, (i + shift) % n) for i in range(n)])
        total = total + moved.astype(jnp.float32)
    return total


def weight_grad_sum(weight_part):
    n_far = lax.axis_size(DP_FAR)
    n_core = lax.axis_size("dp_core")
    blocks = weight_part.reshape(n_far, n_core, weight_part.shape[0] // (n_far * n_core), weight_part.shape[1])
    pair = lax.all_to_all(blocks, "dp_core", 1, 1, tiled=True)
    pair = (pair[:, 0].astype(jnp.float32) + pair[:, 1].astype(jnp.float32)).astype(jnp.bfloat16)
    return jnp.sum(lax.all_to_all(pair, DP_FAR, 0, 0, tiled=True).astype(jnp.float32), axis=0)


def head_forward(queries, key_rows, values):
    score_scale = queries.shape[-1] ** (-0.5)
    scores = jnp.dot(queries, key_rows.T, preferred_element_type=jnp.float32) * score_scale
    row_ids = lax.broadcasted_iota(jnp.int32, scores.shape, 0)
    col_ids = lax.broadcasted_iota(jnp.int32, scores.shape, 1)
    scores = jnp.where(col_ids <= row_ids, scores, -1e30)
    row_max = jnp.max(scores, axis=1, keepdims=True)
    weights = jnp.exp(scores - row_max)
    softmax = weights / jnp.sum(weights, axis=1, keepdims=True)
    soft_low = softmax.astype(jnp.bfloat16)
    attended = jnp.dot(soft_low, values, preferred_element_type=jnp.float32).astype(jnp.bfloat16)
    return (softmax, soft_low, attended)


def head_backward(queries, key_rows, values, softmax, soft_low, attended, grad_head):
    score_scale = queries.shape[-1] ** (-0.5)
    row_dot = jnp.sum(
        grad_head.astype(jnp.float32) * attended.astype(jnp.float32), axis=1, keepdims=True
    )
    grad_values = jnp.dot(soft_low.T, grad_head, preferred_element_type=jnp.float32)
    grad_probs = jnp.dot(grad_head, values.T, preferred_element_type=jnp.float32)
    grad_scores = (softmax * (grad_probs - row_dot)).astype(jnp.bfloat16)
    grad_query = jnp.dot(grad_scores, key_rows, preferred_element_type=jnp.float32) * score_scale
    grad_keys = jnp.dot(grad_scores.T, queries, preferred_element_type=jnp.float32) * score_scale
    return jnp.concatenate([grad_query, grad_keys, grad_values], axis=1).astype(jnp.bfloat16)


def body(grad_out, qkv_saved, w_out, w_qkv, plan):
    gradients = grad_out[0, :, 0]
    saved_qkv = qkv_saved[0, :, 0, :, 0]
    out_proj = w_out[0, :, 0]
    qkv_proj = w_qkv[0, :, 0]
    head_size = out_proj.shape[1]
    queries = saved_qkv[:, :, :head_size]
    key_rows = saved_qkv[:, :, head_size : 2 * head_size]
    values = saved_qkv[:, :, 2 * head_size :]
    softmax, soft_low, attended = jax.vmap(head_forward)(queries, key_rows, values)
    weight_part = jnp.einsum("msc,msh->ch", gradients, attended, preferred_element_type=jnp.float32)
    weight_part = with_layout_constraint(weight_part.astype(jnp.bfloat16), Layout((0, 1)))
    weight_grad = weight_grad_sum(weight_part)
    current = plan[0, :BMICRO]
    grad_rows = jnp.stack([lax.dynamic_index_in_dim(gradients, current[j], 0, keepdims=False) for j in range(BMICRO)])
    grad_heads = jnp.einsum(
        "msd,dh->msh", grad_rows, out_proj, preferred_element_type=jnp.float32
    ).astype(jnp.bfloat16)
    grad_qkv = jax.vmap(head_backward)(
        jnp.take(queries, current, axis=0),
        jnp.take(key_rows, current, axis=0),
        jnp.take(values, current, axis=0),
        jnp.take(softmax, current, axis=0),
        jnp.take(soft_low, current, axis=0),
        jnp.take(attended, current, axis=0),
        grad_heads,
    )
    n_tensor = lax.axis_size("tensor")
    seq_len = grad_qkv.shape[1]
    start = lax.axis_index("tensor") * (seq_len // n_tensor)
    grad_qkv = lax.dynamic_slice_in_dim(jnp.concatenate([grad_qkv, grad_qkv], axis=1), start, seq_len, axis=1)
    grouped = grad_qkv.reshape(grad_qkv.shape[0], n_tensor, seq_len // n_tensor, grad_qkv.shape[2])
    partials = jnp.einsum("bjsk,dk->jsbd", grouped, qkv_proj, preferred_element_type=jnp.float32)
    own_rows = rotated_sum(partials.astype(jnp.bfloat16), "tensor")
    received = shifted(own_rows.astype(jnp.bfloat16), "pipe", -1)
    weight_grad = with_layout_constraint(weight_grad[None, :, None, :], Layout((0, 1, 2, 3)))
    return (received[None, None], weight_grad)


def solution(mesh):
    n_pipe, n_dp, n_tensor = (mesh.shape[a] for a in ("pipe", "dp", "tensor"))
    n_y = 2
    n_core = 2
    parts = mesh.devices.reshape(n_pipe, n_y, n_dp // (n_y * n_core), n_core, n_tensor)
    staged = Mesh(parts, ("pipe", *DP_PARTS, "tensor"))
    in_specs = (
        P("pipe", None, DP_PARTS, None, None),
        P("pipe", None, DP_PARTS, None, "tensor", None),
        P("pipe", None, "tensor", None),
        P("pipe", None, "tensor", None),
        P("pipe", None),
    )
    out_specs = (P("pipe", DP_PARTS, "tensor", None, None), P("pipe", DP_PARTS, "tensor", None))
    return jax.shard_map(body, mesh=staged, in_specs=in_specs, out_specs=out_specs, check_vma=False)
```

```python
import jax
import jax.numpy as jnp
from jax import lax
from jax.experimental.layout import Layout, with_layout_constraint
from jax.sharding import Mesh, PartitionSpec as P

BMICRO = 2
DP_PARTS = ("dp_y", "dp_z", "dp_core")
DP_FAR = ("dp_y", "dp_z")


def shifted(block, axis, distance):
    devices = range(lax.axis_size(axis))
    route = [(i - distance, i) for i in devices if i - distance in devices]
    return lax.ppermute(block, axis, route)


def exchange(block, axis):
    n = lax.axis_size(axis)
    parts = block.reshape(n, block.shape[0] // n, *block.shape[1:])
    return lax.all_to_all(parts, axis, 0, 0, tiled=True)


def ordered_sum(parts):
    total = parts[0].astype(jnp.float32)
    for index in range(1, parts.shape[0]):
        total = total + parts[index].astype(jnp.float32)
    return total


def rotated_sum(parts, axis):
    n = parts.shape[0]
    total = parts[0].astype(jnp.float32)
    for shift in range(1, n):
        moved = lax.ppermute(parts[shift], axis, [(i, (i + shift) % n) for i in range(n)])
        total = total + moved.astype(jnp.float32)
    return total


def weight_grad_sum(weight_part):
    n_far = lax.axis_size(DP_FAR)
    n_core = lax.axis_size("dp_core")
    blocks = weight_part.reshape(n_far, n_core, weight_part.shape[0] // (n_far * n_core), weight_part.shape[1])
    pair = lax.all_to_all(blocks, "dp_core", 1, 1, tiled=True)
    pair = (pair[:, 0].astype(jnp.float32) + pair[:, 1].astype(jnp.float32)).astype(jnp.bfloat16)
    return jnp.sum(lax.all_to_all(pair, DP_FAR, 0, 0, tiled=True).astype(jnp.float32), axis=0)


def head_forward(queries, key_rows, values):
    score_scale = queries.shape[-1] ** (-0.5)
    scores = jnp.dot(queries, key_rows.T, preferred_element_type=jnp.float32) * score_scale
    row_ids = lax.broadcasted_iota(jnp.int32, scores.shape, 0)
    col_ids = lax.broadcasted_iota(jnp.int32, scores.shape, 1)
    scores = jnp.where(col_ids <= row_ids, scores, -1e30)
    row_max = jnp.max(scores, axis=1, keepdims=True)
    weights = jnp.exp(scores - row_max)
    softmax = weights / jnp.sum(weights, axis=1, keepdims=True)
    soft_low = softmax.astype(jnp.bfloat16)
    attended = jnp.dot(soft_low, values, preferred_element_type=jnp.float32).astype(jnp.bfloat16)
    return (softmax, soft_low, attended)


def head_backward(queries, key_rows, values, softmax, soft_low, attended, grad_head):
    score_scale = queries.shape[-1] ** (-0.5)
    row_dot = jnp.sum(
        grad_head.astype(jnp.float32) * attended.astype(jnp.float32), axis=1, keepdims=True
    )
    grad_values = jnp.dot(soft_low.T, grad_head, preferred_element_type=jnp.float32)
    grad_probs = jnp.dot(grad_head, values.T, preferred_element_type=jnp.float32)
    grad_scores = (softmax * (grad_probs - row_dot)).astype(jnp.bfloat16)
    grad_query = jnp.dot(grad_scores, key_rows, preferred_element_type=jnp.float32) * score_scale
    grad_keys = jnp.dot(grad_scores.T, queries, preferred_element_type=jnp.float32) * score_scale
    return jnp.concatenate([grad_query, grad_keys, grad_values], axis=1).astype(jnp.bfloat16)


def body(grad_out, qkv_saved, w_out, w_qkv, plan):
    gradients = grad_out[0, :, 0]
    saved_qkv = qkv_saved[0, :, 0, :, 0]
    out_proj = w_out[0, :, 0]
    qkv_proj = w_qkv[0, :, 0]
    head_size = out_proj.shape[1]
    queries = saved_qkv[:, :, :head_size]
    key_rows = saved_qkv[:, :, head_size : 2 * head_size]
    values = saved_qkv[:, :, 2 * head_size :]
    softmax, soft_low, attended = jax.vmap(head_forward)(queries, key_rows, values)
    weight_part = jnp.einsum("msc,msh->ch", gradients, attended, preferred_element_type=jnp.float32)
    weight_part = with_layout_constraint(weight_part.astype(jnp.bfloat16), Layout((0, 1)))
    weight_grad = weight_grad_sum(weight_part)
    current = plan[0, :BMICRO]
    grad_heads = jnp.einsum(
        "msd,dh->msh", gradients, out_proj, preferred_element_type=jnp.float32
    ).astype(jnp.bfloat16)
    grad_qkv = jax.vmap(head_backward)(
        jnp.take(queries, current, axis=0),
        jnp.take(key_rows, current, axis=0),
        jnp.take(values, current, axis=0),
        jnp.take(softmax, current, axis=0),
        jnp.take(soft_low, current, axis=0),
        jnp.take(attended, current, axis=0),
        jnp.take(grad_heads, current, axis=0),
    )
    n_tensor = lax.axis_size("tensor")
    seq_len = grad_qkv.shape[1]
    start = lax.axis_index("tensor") * (seq_len // n_tensor)
    grad_qkv = lax.dynamic_slice_in_dim(jnp.concatenate([grad_qkv, grad_qkv], axis=1), start, seq_len, axis=1)
    grouped = grad_qkv.reshape(grad_qkv.shape[0], n_tensor, seq_len // n_tensor, grad_qkv.shape[2])
    partials = jnp.einsum("bjsk,dk->jsbd", grouped, qkv_proj, preferred_element_type=jnp.float32)
    own_rows = rotated_sum(partials.astype(jnp.bfloat16), "tensor")
    received = shifted(own_rows.astype(jnp.bfloat16), "pipe", -1)
    weight_grad = with_layout_constraint(weight_grad[None, :, None, :], Layout((0, 1, 2, 3)))
    return (received[None, None], weight_grad)


def solution(mesh):
    n_pipe, n_dp, n_tensor = (mesh.shape[a] for a in ("pipe", "dp", "tensor"))
    n_y = 2
    n_core = 2
    parts = mesh.devices.reshape(n_pipe, n_y, n_dp // (n_y * n_core), n_core, n_tensor)
    staged = Mesh(parts, ("pipe", *DP_PARTS, "tensor"))
    in_specs = (
        P("pipe", None, DP_PARTS, None, None),
        P("pipe", None, DP_PARTS, None, "tensor", None),
        P("pipe", None, "tensor", None),
        P("pipe", None, "tensor", None),
        P("pipe", None),
    )
    out_specs = (P("pipe", DP_PARTS, "tensor", None, None), P("pipe", DP_PARTS, "tensor", None))
    return jax.shard_map(body, mesh=staged, in_specs=in_specs, out_specs=out_specs, check_vma=False)
```

```python
import jax
import jax.numpy as jnp
from jax import lax
from jax.experimental.layout import Layout, with_layout_constraint
from jax.sharding import Mesh, PartitionSpec as P

BMICRO = 2
DP_PARTS = ("dp_y", "dp_z", "dp_core")
DP_FAR = ("dp_y", "dp_z")


def shifted(block, axis, distance):
    devices = range(lax.axis_size(axis))
    route = [(i - distance, i) for i in devices if i - distance in devices]
    return lax.ppermute(block, axis, route)


def exchange(block, axis):
    n = lax.axis_size(axis)
    parts = block.reshape(n, block.shape[0] // n, *block.shape[1:])
    return lax.all_to_all(parts, axis, 0, 0, tiled=True)


def ordered_sum(parts):
    total = parts[0].astype(jnp.float32)
    for index in range(1, parts.shape[0]):
        total = total + parts[index].astype(jnp.float32)
    return total


def rotated_sum(parts, axis):
    n = parts.shape[0]
    total = parts[0].astype(jnp.float32)
    for shift in range(1, n):
        moved = lax.ppermute(parts[shift], axis, [(i, (i + shift) % n) for i in range(n)])
        total = total + moved.astype(jnp.float32)
    return total


def weight_grad_sum(weight_part):
    n_far = lax.axis_size(DP_FAR)
    n_core = lax.axis_size("dp_core")
    blocks = weight_part.reshape(n_far, n_core, weight_part.shape[0] // (n_far * n_core), weight_part.shape[1])
    pair = lax.all_to_all(blocks, "dp_core", 1, 1, tiled=True)
    pair = (pair[:, 0].astype(jnp.float32) + pair[:, 1].astype(jnp.float32)).astype(jnp.bfloat16)
    return jnp.sum(lax.all_to_all(pair, DP_FAR, 0, 0, tiled=True).astype(jnp.float32), axis=0)


def head_forward(queries, key_rows, values):
    score_scale = queries.shape[-1] ** (-0.5)
    scores = jnp.dot(queries, key_rows.T, preferred_element_type=jnp.float32) * score_scale
    row_ids = lax.broadcasted_iota(jnp.int32, scores.shape, 0)
    col_ids = lax.broadcasted_iota(jnp.int32, scores.shape, 1)
    scores = jnp.where(col_ids <= row_ids, scores, -1e30)
    row_max = jnp.max(scores, axis=1, keepdims=True)
    weights = jnp.exp(scores - row_max)
    softmax = weights / jnp.sum(weights, axis=1, keepdims=True)
    soft_low = softmax.astype(jnp.bfloat16)
    attended = jnp.dot(soft_low, values, preferred_element_type=jnp.float32).astype(jnp.bfloat16)
    return (softmax, soft_low, attended)


def head_backward(queries, key_rows, values, softmax, soft_low, attended, grad_head):
    score_scale = queries.shape[-1] ** (-0.5)
    row_dot = jnp.sum(
        grad_head.astype(jnp.float32) * attended.astype(jnp.float32), axis=1, keepdims=True
    )
    grad_values = jnp.dot(soft_low.T, grad_head, preferred_element_type=jnp.float32)
    grad_probs = jnp.dot(grad_head, values.T, preferred_element_type=jnp.float32)
    grad_scores = (softmax * (grad_probs - row_dot)).astype(jnp.bfloat16)
    grad_query = jnp.dot(grad_scores, key_rows, preferred_element_type=jnp.float32) * score_scale
    grad_keys = jnp.dot(grad_scores.T, queries, preferred_element_type=jnp.float32) * score_scale
    return jnp.concatenate([grad_query, grad_keys, grad_values], axis=1).astype(jnp.bfloat16)


def body(grad_out, qkv_saved, w_out, w_qkv, plan):
    gradients = grad_out[0, :, 0]
    saved_qkv = qkv_saved[0, :, 0, :, 0]
    out_proj = w_out[0, :, 0]
    qkv_proj = w_qkv[0, :, 0]
    head_size = out_proj.shape[1]
    queries = saved_qkv[:, :, :head_size]
    key_rows = saved_qkv[:, :, head_size : 2 * head_size]
    values = saved_qkv[:, :, 2 * head_size :]
    softmax, soft_low, attended = jax.vmap(head_forward)(queries, key_rows, values)
    weight_part = jnp.einsum("msc,msh->ch", gradients, attended, preferred_element_type=jnp.float32)
    weight_part = with_layout_constraint(weight_part.astype(jnp.bfloat16), Layout((0, 1)))
    weight_grad = weight_grad_sum(weight_part)
    current = plan[0, :BMICRO]
    grad_heads = jnp.einsum(
        "msd,dh->msh", gradients, out_proj, preferred_element_type=jnp.float32
    ).astype(jnp.bfloat16)
    grad_qkv = jax.vmap(head_backward)(queries, key_rows, values, softmax, soft_low, attended, grad_heads)
    grad_qkv = jnp.take(grad_qkv, current, axis=0)
    n_tensor = lax.axis_size("tensor")
    seq_len = grad_qkv.shape[1]
    start = lax.axis_index("tensor") * (seq_len // n_tensor)
    grad_qkv = lax.dynamic_slice_in_dim(jnp.concatenate([grad_qkv, grad_qkv], axis=1), start, seq_len, axis=1)
    grouped = grad_qkv.reshape(grad_qkv.shape[0], n_tensor, seq_len // n_tensor, grad_qkv.shape[2])
    partials = jnp.einsum("bjsk,dk->jsbd", grouped, qkv_proj, preferred_element_type=jnp.float32)
    own_rows = rotated_sum(partials.astype(jnp.bfloat16), "tensor")
    received = shifted(own_rows.astype(jnp.bfloat16), "pipe", -1)
    return (received[None, None], weight_grad[None, :, None, :])


def solution(mesh):
    n_pipe, n_dp, n_tensor = (mesh.shape[a] for a in ("pipe", "dp", "tensor"))
    n_y = 2
    n_core = 2
    parts = mesh.devices.reshape(n_pipe, n_y, n_dp // (n_y * n_core), n_core, n_tensor)
    staged = Mesh(parts, ("pipe", *DP_PARTS, "tensor"))
    in_specs = (
        P("pipe", None, DP_PARTS, None, None),
        P("pipe", None, DP_PARTS, None, "tensor", None),
        P("pipe", None, "tensor", None),
        P("pipe", None, "tensor", None),
        P("pipe", None),
    )
    out_specs = (P("pipe", DP_PARTS, "tensor", None, None), P("pipe", DP_PARTS, "tensor", None))
    return jax.shard_map(body, mesh=staged, in_specs=in_specs, out_specs=out_specs, check_vma=False)
```

```python
import jax
import jax.numpy as jnp
from jax import lax
from jax.experimental.layout import Layout, with_layout_constraint
from jax.sharding import Mesh, PartitionSpec as P

BMICRO = 2
DP_PARTS = ("dp_y", "dp_z", "dp_core")
DP_FAR = ("dp_y", "dp_z")


def shifted(block, axis, distance):
    devices = range(lax.axis_size(axis))
    route = [(i - distance, i) for i in devices if i - distance in devices]
    return lax.ppermute(block, axis, route)


def exchange(block, axis):
    n = lax.axis_size(axis)
    parts = block.reshape(n, block.shape[0] // n, *block.shape[1:])
    return lax.all_to_all(parts, axis, 0, 0, tiled=True)


def ordered_sum(parts):
    total = parts[0].astype(jnp.float32)
    for index in range(1, parts.shape[0]):
        total = total + parts[index].astype(jnp.float32)
    return total


def rotated_sum(parts, axis):
    n = len(parts)
    total = parts[0].astype(jnp.float32)
    for shift in range(1, n):
        moved = lax.ppermute(parts[shift], axis, [(i, (i + shift) % n) for i in range(n)])
        total = total + moved.astype(jnp.float32)
    return total


def weight_grad_sum(weight_part):
    n_far = lax.axis_size(DP_FAR)
    n_core = lax.axis_size("dp_core")
    blocks = weight_part.reshape(n_far, n_core, weight_part.shape[0] // (n_far * n_core), weight_part.shape[1])
    pair = lax.all_to_all(blocks, "dp_core", 1, 1, tiled=True)
    pair = (pair[:, 0].astype(jnp.float32) + pair[:, 1].astype(jnp.float32)).astype(jnp.bfloat16)
    return jnp.sum(lax.all_to_all(pair, DP_FAR, 0, 0, tiled=True).astype(jnp.float32), axis=0)


def head_forward(queries, key_rows, values):
    score_scale = queries.shape[-1] ** (-0.5)
    scores = jnp.dot(queries, key_rows.T, preferred_element_type=jnp.float32) * score_scale
    row_ids = lax.broadcasted_iota(jnp.int32, scores.shape, 0)
    col_ids = lax.broadcasted_iota(jnp.int32, scores.shape, 1)
    scores = jnp.where(col_ids <= row_ids, scores, -1e30)
    row_max = jnp.max(scores, axis=1, keepdims=True)
    weights = jnp.exp(scores - row_max)
    softmax = weights / jnp.sum(weights, axis=1, keepdims=True)
    soft_low = softmax.astype(jnp.bfloat16)
    attended = jnp.dot(soft_low, values, preferred_element_type=jnp.float32).astype(jnp.bfloat16)
    return (softmax, soft_low, attended)


def head_backward(queries, key_rows, values, softmax, soft_low, attended, grad_head):
    score_scale = queries.shape[-1] ** (-0.5)
    row_dot = jnp.sum(
        grad_head.astype(jnp.float32) * attended.astype(jnp.float32), axis=1, keepdims=True
    )
    grad_values = jnp.dot(soft_low.T, grad_head, preferred_element_type=jnp.float32)
    grad_probs = jnp.dot(grad_head, values.T, preferred_element_type=jnp.float32)
    grad_scores = (softmax * (grad_probs - row_dot)).astype(jnp.bfloat16)
    grad_query = jnp.dot(grad_scores, key_rows, preferred_element_type=jnp.float32) * score_scale
    grad_keys = jnp.dot(grad_scores.T, queries, preferred_element_type=jnp.float32) * score_scale
    return jnp.concatenate([grad_query, grad_keys, grad_values], axis=1).astype(jnp.bfloat16)


def body(grad_out, qkv_saved, w_out, w_qkv, plan):
    gradients = grad_out[0, :, 0]
    saved_qkv = qkv_saved[0, :, 0, :, 0]
    out_proj = w_out[0, :, 0]
    qkv_proj = w_qkv[0, :, 0]
    head_size = out_proj.shape[1]
    queries = saved_qkv[:, :, :head_size]
    key_rows = saved_qkv[:, :, head_size : 2 * head_size]
    values = saved_qkv[:, :, 2 * head_size :]
    softmax, soft_low, attended = jax.vmap(head_forward)(queries, key_rows, values)
    weight_part = jnp.einsum("msc,msh->ch", gradients, attended, preferred_element_type=jnp.float32)
    weight_part = with_layout_constraint(weight_part.astype(jnp.bfloat16), Layout((0, 1)))
    weight_grad = weight_grad_sum(weight_part)
    current = plan[0, :BMICRO]
    grad_heads = jnp.einsum(
        "msd,dh->msh", gradients, out_proj, preferred_element_type=jnp.float32
    ).astype(jnp.bfloat16)
    grad_qkv = jax.vmap(head_backward)(queries, key_rows, values, softmax, soft_low, attended, grad_heads)
    grad_qkv = jnp.take(grad_qkv, current, axis=0)
    n_tensor = lax.axis_size("tensor")
    seq_len = grad_qkv.shape[1]
    start = lax.axis_index("tensor") * (seq_len // n_tensor)
    grad_qkv = lax.dynamic_slice_in_dim(jnp.concatenate([grad_qkv, grad_qkv], axis=1), start, seq_len, axis=1)
    grouped = grad_qkv.reshape(grad_qkv.shape[0], n_tensor, seq_len // n_tensor, grad_qkv.shape[2])
    partials = [
        jnp.einsum("bsk,dk->sbd", grouped[:, k], qkv_proj, preferred_element_type=jnp.float32).astype(jnp.bfloat16)
        for k in range(n_tensor)
    ]
    own_rows = rotated_sum(partials, "tensor")
    received = shifted(own_rows.astype(jnp.bfloat16), "pipe", -1)
    return (received[None, None], weight_grad[None, :, None, :])


def solution(mesh):
    n_pipe, n_dp, n_tensor = (mesh.shape[a] for a in ("pipe", "dp", "tensor"))
    n_y = 2
    n_core = 2
    parts = mesh.devices.reshape(n_pipe, n_y, n_dp // (n_y * n_core), n_core, n_tensor)
    staged = Mesh(parts, ("pipe", *DP_PARTS, "tensor"))
    in_specs = (
        P("pipe", None, DP_PARTS, None, None),
        P("pipe", None, DP_PARTS, None, "tensor", None),
        P("pipe", None, "tensor", None),
        P("pipe", None, "tensor", None),
        P("pipe", None),
    )
    out_specs = (P("pipe", DP_PARTS, "tensor", None, None), P("pipe", DP_PARTS, "tensor", None))
    return jax.shard_map(body, mesh=staged, in_specs=in_specs, out_specs=out_specs, check_vma=False)
```

```python
import jax
import jax.numpy as jnp
from jax import lax
from jax.experimental.layout import Layout, with_layout_constraint
from jax.sharding import Mesh, PartitionSpec as P

BMICRO = 2
DP_PARTS = ("dp_y", "dp_z", "dp_core")
DP_FAR = ("dp_y", "dp_z")


def shifted(block, axis, distance):
    devices = range(lax.axis_size(axis))
    route = [(i - distance, i) for i in devices if i - distance in devices]
    return lax.ppermute(block, axis, route)


def exchange(block, axis):
    n = lax.axis_size(axis)
    parts = block.reshape(n, block.shape[0] // n, *block.shape[1:])
    return lax.all_to_all(parts, axis, 0, 0, tiled=True)


def ordered_sum(parts):
    total = parts[0].astype(jnp.float32)
    for index in range(1, parts.shape[0]):
        total = total + parts[index].astype(jnp.float32)
    return total


def rotated_sum(parts, axis):
    n = parts.shape[0]
    total = parts[0].astype(jnp.float32)
    for shift in range(1, n):
        moved = lax.ppermute(parts[shift], axis, [(i, (i + shift) % n) for i in range(n)])
        total = total + moved.astype(jnp.float32)
    return total


def weight_grad_sum(weight_part):
    n_far = lax.axis_size(DP_FAR)
    n_core = lax.axis_size("dp_core")
    blocks = weight_part.reshape(n_far, n_core, weight_part.shape[0] // (n_far * n_core), weight_part.shape[1])
    pair = lax.all_to_all(blocks, "dp_core", 1, 1, tiled=True)
    pair = (pair[:, 0].astype(jnp.float32) + pair[:, 1].astype(jnp.float32)).astype(jnp.bfloat16)
    return jnp.sum(lax.all_to_all(pair, DP_FAR, 0, 0, tiled=True).astype(jnp.float32), axis=0)


def head_forward(queries, key_rows, values):
    score_scale = queries.shape[-1] ** (-0.5)
    scores = jnp.dot(queries, key_rows.T, preferred_element_type=jnp.float32) * score_scale
    row_ids = lax.broadcasted_iota(jnp.int32, scores.shape, 0)
    col_ids = lax.broadcasted_iota(jnp.int32, scores.shape, 1)
    scores = jnp.where(col_ids <= row_ids, scores, -1e30)
    row_max = jnp.max(scores, axis=1, keepdims=True)
    weights = jnp.exp(scores - row_max)
    softmax = weights / jnp.sum(weights, axis=1, keepdims=True)
    soft_low = softmax.astype(jnp.bfloat16)
    attended = jnp.dot(soft_low, values, preferred_element_type=jnp.float32).astype(jnp.bfloat16)
    return (softmax, soft_low, attended)


def head_backward(queries, key_rows, values, softmax, soft_low, attended, grad_head):
    score_scale = queries.shape[-1] ** (-0.5)
    row_dot = jnp.sum(
        grad_head.astype(jnp.float32) * attended.astype(jnp.float32), axis=1, keepdims=True
    )
    grad_values = jnp.dot(soft_low.T, grad_head, preferred_element_type=jnp.float32)
    grad_probs = jnp.dot(grad_head, values.T, preferred_element_type=jnp.float32)
    grad_scores = (softmax * (grad_probs - row_dot)).astype(jnp.bfloat16)
    grad_query = jnp.dot(grad_scores, key_rows, preferred_element_type=jnp.float32) * score_scale
    grad_keys = jnp.dot(grad_scores.T, queries, preferred_element_type=jnp.float32) * score_scale
    return jnp.concatenate([grad_query, grad_keys, grad_values], axis=1).astype(jnp.bfloat16)


def body(grad_out, qkv_saved, w_out, w_qkv, plan):
    gradients = grad_out[0, :, 0]
    saved_qkv = qkv_saved[0, :, 0, :, 0]
    out_proj = w_out[0, :, 0]
    qkv_proj = w_qkv[0, :, 0]
    head_size = out_proj.shape[1]
    queries = saved_qkv[:, :, :head_size]
    key_rows = saved_qkv[:, :, head_size : 2 * head_size]
    values = saved_qkv[:, :, 2 * head_size :]
    softmax, soft_low, attended = jax.vmap(head_forward)(queries, key_rows, values)
    weight_part = jnp.einsum("msc,msh->ch", gradients, attended, preferred_element_type=jnp.float32)
    weight_part = with_layout_constraint(weight_part.astype(jnp.bfloat16), Layout((0, 1)))
    weight_grad = weight_grad_sum(weight_part)
    current = plan[0, :BMICRO]
    grad_heads = jnp.einsum(
        "msd,dh->msh", gradients, out_proj, preferred_element_type=jnp.float32
    ).astype(jnp.bfloat16)
    grad_qkv = jax.vmap(head_backward)(queries, key_rows, values, softmax, soft_low, attended, grad_heads)
    grad_qkv = jnp.take(grad_qkv, current, axis=0)
    n_tensor = lax.axis_size("tensor")
    seq_len = grad_qkv.shape[1]
    start = lax.axis_index("tensor") * (seq_len // n_tensor)
    grad_qkv = lax.dynamic_slice_in_dim(jnp.concatenate([grad_qkv, grad_qkv], axis=1), start, seq_len, axis=1)
    grouped = grad_qkv.reshape(grad_qkv.shape[0], n_tensor, seq_len // n_tensor, grad_qkv.shape[2])
    partials = jnp.einsum("bjsk,dk->jsbd", grouped, qkv_proj, preferred_element_type=jnp.float32)
    own_rows = rotated_sum(partials.astype(jnp.bfloat16), "tensor")
    received = shifted(own_rows.astype(jnp.bfloat16), "pipe", -1)
    weight_grad = with_layout_constraint(weight_grad[None, :, None, :], Layout((0, 1, 2, 3)))
    return (received[None, None], weight_grad)


def solution(mesh):
    n_pipe, n_dp, n_tensor = (mesh.shape[a] for a in ("pipe", "dp", "tensor"))
    n_y = 2
    n_core = 2
    parts = mesh.devices.reshape(n_pipe, n_y, n_dp // (n_y * n_core), n_core, n_tensor)
    staged = Mesh(parts, ("pipe", *DP_PARTS, "tensor"))
    in_specs = (
        P("pipe", None, DP_PARTS, None, None),
        P("pipe", None, DP_PARTS, None, "tensor", None),
        P("pipe", None, "tensor", None),
        P("pipe", None, "tensor", None),
        P("pipe", None),
    )
    out_specs = (P("pipe", DP_PARTS, "tensor", None, None), P("pipe", DP_PARTS, "tensor", None))
    return jax.shard_map(body, mesh=staged, in_specs=in_specs, out_specs=out_specs, check_vma=False)
```

```python
import jax
import jax.numpy as jnp
from jax import lax
from jax.experimental.layout import Layout, with_layout_constraint
from jax.sharding import Mesh, PartitionSpec as P

BMICRO = 2
DP_PARTS = ("dp_y", "dp_z", "dp_core")
DP_FAR = ("dp_y", "dp_z")


def shifted(block, axis, distance):
    devices = range(lax.axis_size(axis))
    route = [(i - distance, i) for i in devices if i - distance in devices]
    return lax.ppermute(block, axis, route)


def exchange(block, axis):
    n = lax.axis_size(axis)
    parts = block.reshape(n, block.shape[0] // n, *block.shape[1:])
    return lax.all_to_all(parts, axis, 0, 0, tiled=True)


def ordered_sum(parts):
    total = parts[0].astype(jnp.float32)
    for index in range(1, parts.shape[0]):
        total = total + parts[index].astype(jnp.float32)
    return total


def rotated_sum(parts, axis):
    n = parts.shape[0]
    total = parts[0].astype(jnp.float32)
    for shift in range(1, n):
        moved = lax.ppermute(parts[shift], axis, [(i, (i + shift) % n) for i in range(n)])
        total = total + moved.astype(jnp.float32)
    return total


def weight_grad_sum(weight_part):
    n_far = lax.axis_size(DP_FAR)
    n_core = lax.axis_size("dp_core")
    blocks = weight_part.reshape(n_far, n_core, weight_part.shape[0] // (n_far * n_core), weight_part.shape[1])
    pair = lax.all_to_all(blocks, "dp_core", 1, 1, tiled=True)
    pair = (pair[:, 0].astype(jnp.float32) + pair[:, 1].astype(jnp.float32)).astype(jnp.bfloat16)
    return jnp.sum(lax.all_to_all(pair, DP_FAR, 0, 0, tiled=True).astype(jnp.float32), axis=0)


def head_forward(queries, key_rows, values):
    score_scale = queries.shape[-1] ** (-0.5)
    scores = jnp.dot(queries, key_rows.T, preferred_element_type=jnp.float32) * score_scale
    row_ids = lax.broadcasted_iota(jnp.int32, scores.shape, 0)
    col_ids = lax.broadcasted_iota(jnp.int32, scores.shape, 1)
    scores = jnp.where(col_ids <= row_ids, scores, -1e30)
    row_max = jnp.max(scores, axis=1, keepdims=True)
    weights = jnp.exp(scores - row_max)
    softmax = weights / jnp.sum(weights, axis=1, keepdims=True)
    soft_low = softmax.astype(jnp.bfloat16)
    attended = jnp.dot(soft_low, values, preferred_element_type=jnp.float32).astype(jnp.bfloat16)
    return (softmax, soft_low, attended)


def head_backward(queries, key_rows, values, softmax, soft_low, attended, grad_head):
    score_scale = queries.shape[-1] ** (-0.5)
    row_dot = jnp.sum(
        grad_head.astype(jnp.float32) * attended.astype(jnp.float32), axis=1, keepdims=True
    )
    grad_values = jnp.dot(soft_low.T, grad_head, preferred_element_type=jnp.float32)
    grad_probs = jnp.dot(grad_head, values.T, preferred_element_type=jnp.float32)
    grad_scores = (softmax * (grad_probs - row_dot)).astype(jnp.bfloat16)
    grad_query = jnp.dot(grad_scores, key_rows, preferred_element_type=jnp.float32) * score_scale
    grad_keys = jnp.dot(grad_scores.T, queries, preferred_element_type=jnp.float32) * score_scale
    return jnp.concatenate([grad_query, grad_keys, grad_values], axis=1).astype(jnp.bfloat16)


def body(grad_out, qkv_saved, w_out, w_qkv, plan):
    gradients = grad_out[0, :, 0]
    saved_qkv = qkv_saved[0, :, 0, :, 0]
    out_proj = w_out[0, :, 0]
    qkv_proj = w_qkv[0, :, 0]
    head_size = out_proj.shape[1]
    queries = saved_qkv[:, :, :head_size]
    key_rows = saved_qkv[:, :, head_size : 2 * head_size]
    values = saved_qkv[:, :, 2 * head_size :]
    softmax, soft_low, attended = jax.vmap(head_forward)(queries, key_rows, values)
    weight_part = jnp.einsum("msc,msh->ch", gradients, attended, preferred_element_type=jnp.float32)
    weight_part = with_layout_constraint(weight_part.astype(jnp.bfloat16), Layout((0, 1)))
    weight_grad = weight_grad_sum(weight_part)
    current = plan[0, :BMICRO]
    grad_heads = jnp.einsum(
        "msd,dh->msh", gradients, out_proj, preferred_element_type=jnp.float32
    ).astype(jnp.bfloat16)
    grad_qkv = jax.vmap(head_backward)(queries, key_rows, values, softmax, soft_low, attended, grad_heads)
    grad_qkv = jnp.take(grad_qkv, current, axis=0, mode="clip")
    n_tensor = lax.axis_size("tensor")
    seq_len = grad_qkv.shape[1]
    start = lax.axis_index("tensor") * (seq_len // n_tensor)
    grad_qkv = lax.dynamic_slice_in_dim(jnp.concatenate([grad_qkv, grad_qkv], axis=1), start, seq_len, axis=1)
    grouped = grad_qkv.reshape(grad_qkv.shape[0], n_tensor, seq_len // n_tensor, grad_qkv.shape[2])
    partials = jnp.einsum("bjsk,dk->jsbd", grouped, qkv_proj, preferred_element_type=jnp.float32)
    own_rows = rotated_sum(partials.astype(jnp.bfloat16), "tensor")
    received = shifted(own_rows.astype(jnp.bfloat16), "pipe", -1)
    return (received[None, None], weight_grad[None, :, None, :])


def solution(mesh):
    n_pipe, n_dp, n_tensor = (mesh.shape[a] for a in ("pipe", "dp", "tensor"))
    n_y = 2
    n_core = 2
    parts = mesh.devices.reshape(n_pipe, n_y, n_dp // (n_y * n_core), n_core, n_tensor)
    staged = Mesh(parts, ("pipe", *DP_PARTS, "tensor"))
    in_specs = (
        P("pipe", None, DP_PARTS, None, None),
        P("pipe", None, DP_PARTS, None, "tensor", None),
        P("pipe", None, "tensor", None),
        P("pipe", None, "tensor", None),
        P("pipe", None),
    )
    out_specs = (P("pipe", DP_PARTS, "tensor", None, None), P("pipe", DP_PARTS, "tensor", None))
    return jax.shard_map(body, mesh=staged, in_specs=in_specs, out_specs=out_specs, check_vma=False)
```
